256 devices in a mesh: space: 32 (over z, x), section: 4 (over y), rep: 2 (over core).
Axes of the slice: x: 4, y: 4, z: 8, core: 2. Of those that a mesh axis runs over, the one named last changes fastest.
Arguments:
- feats: bfloat16 [4, 128, 40, 256], P('rep', 'space'), may hold values from -6 to 6
- labels: int32 [4, 128, 40], P('rep', 'space'), may hold values from 0 to 2
- class_weight: int32 [3], replicated, may hold values from 1 to 9
- depth_kernel: bfloat16 [4, 3, 9, 256], P('section'), may hold values from -2 to 2
- point_weight: bfloat16 [4, 4, 256, 256], P('section'), may hold values from -0.375 to 0.375
- proj_weight: bfloat16 [4, 1024, 256], P('section'), may hold values from -0.1875 to 0.1875
- head_weight: bfloat16 [4, 256, 3], P('section'), may hold values from -0.375 to 0.375
Outputs:
- kernel_grad: float32 [4, 3, 9, 256], P('section')
- point_grad: float32 [4, 4, 256, 256], P('section')
- proj_grad: float32 [4, 1024, 256], P('section')
- head_grad: float32 [4, 256, 3], P('section')
The draws below stay inside these ranges and needn't reach their ends.
All inputs are finite; a program needn't handle non-finite values.
Results may differ from the reference program's by a relative error of at most 0.013.
The reference program's roundings to bfloat16 on the way count: a program that leaves them out, or rounds other values in their place, can miss the bound.
Values may be sent and summed in bfloat16 or wider, within the bound.
No kernel may reach another device: no remote copies, remote signals or barrier semaphores. Data moves between devices by JAX's collectives and lax.ppermute only.
A program may use at most 128 MiB of HBM per device.

```python
import jax
import jax.numpy as jnp
from jax import lax

C = 256
COLS = 40
SECTIONS = 4
H = 128
SNAPS = 4


def with_ends(values, key, smallest, top_value):
    longest = values.shape.index(max(values.shape))
    spots = []
    for shift in (0, 1):
        where = [jax.random.randint(jax.random.fold_in(key, axis), (), 0, length) for axis, length in enumerate(values.shape)]
        where[longest] = (where[longest] + shift) % values.shape[longest]
        spots.append(tuple(where))
    return values.at[spots[0]].set(smallest).at[spots[1]].set(top_value)


def levels(rng, extent, split, low, top_value):
    loudness = 1.0
    for position, blocks in split:
        heights = jax.random.uniform(jax.random.fold_in(jax.random.fold_in(rng, 6), position), (blocks,), jnp.float32, low / len(split), top_value / len(split))
        loudness = loudness * jnp.repeat(jnp.exp(heights), extent[position] // blocks).reshape((-1,) + (1,) * (len(extent) - 1 - position))
    return loudness


def noise(rng, shape, width, bound, cuts=(), kind=jnp.bfloat16):
    gain = levels(rng, shape, cuts, -0.22, 0.18) if cuts else 1.0
    values = jax.random.normal(rng, shape, jnp.float32) * width * gain
    return jnp.minimum(jnp.maximum(values, -bound), bound).astype(kind)


def setup_inputs(seed: int = 0) -> dict:
    key_of = jax.random.split(jax.random.key(seed), 8)
    feats = noise(key_of[0], (SNAPS, H, COLS, C), 1.0, 6.0, ((0, 2), (1, 32)))
    labels = with_ends(jax.random.randint(key_of[1], (SNAPS, H, COLS), 0, 3), jax.random.fold_in(key_of[1], 1), 0, 2).astype(jnp.int32)
    class_weight = jax.random.randint(key_of[2], (3,), 1, 10).astype(jnp.int32)
    depth_kernel = noise(key_of[3], (SECTIONS, 3, 9, C), 9 ** -0.5, 2.0, ((0, 4),))
    point_weight = noise(key_of[4], (SECTIONS, 4, C, C), C ** -0.5, 0.375, ((0, 4),))
    proj_weight = noise(key_of[5], (SECTIONS, 4 * C, C), (4 * C) ** -0.5, 0.1875, ((0, 4),))
    head_weight = noise(key_of[6], (SECTIONS, C, 3), C ** -0.5, 0.375, ((0, 4),))
    return dict(feats=feats, labels=labels, class_weight=class_weight, depth_kernel=depth_kernel, point_weight=point_weight, proj_weight=proj_weight, head_weight=head_weight)


spacings = (12, 24, 36)
loss_scale = 256.0


def moved(source, offset, axis_dim):
    length = source.shape[axis_dim]
    if abs(offset) >= length:
        return jnp.zeros_like(source)
    widths = [(0, 0)] * source.ndim
    widths[axis_dim] = (max(-offset, 0), max(offset, 0))
    padded = jnp.pad(source, widths)
    begin_at = max(offset, 0)
    return lax.slice_in_dim(padded, begin_at, begin_at + length, axis=axis_dim)


def depthwise(source, tap_weights, spacing):
    running = jnp.zeros(source.shape, jnp.float32)
    for row_tap in (-1, 0, 1):
        row_moved = moved(source, row_tap * spacing, 0)
        for col_tap in (-1, 0, 1):
            running = running + tap_weights[3 * (row_tap + 1) + col_tap + 1] * moved(row_moved, col_tap * spacing, 1)
    return running


def depthwise_back(grads, base_map, tap_weights, spacing):
    running = jnp.zeros(grads.shape, jnp.float32)
    kernel_rows = []
    for row_tap in (-1, 0, 1):
        row_moved = moved(grads, -row_tap * spacing, 0)
        for col_tap in (-1, 0, 1):
            shifted = moved(row_moved, -col_tap * spacing, 1)
            running = running + tap_weights[3 * (row_tap + 1) + col_tap + 1] * shifted
            kernel_rows.append(jnp.sum(shifted * base_map, axis=(0, 1)))
    return running, jnp.stack(kernel_rows)


def matmul(first_op, second_op):
    return jnp.dot(first_op, second_op, preferred_element_type=jnp.float32)


def outer(first_op, second_op):
    return lax.dot_general(first_op, second_op, (((0,), (0,)), ((), ())), preferred_element_type=jnp.float32)


def reference(feats, labels, class_weight, depth_kernel, point_weight, proj_weight, head_weight):
    pixels = H * COLS
    factor = loss_scale / (SNAPS * H * COLS)
    weight_table = class_weight.astype(jnp.float32)
    class_ids = jnp.arange(3, dtype=jnp.int32)
    kernel_acc = [jnp.zeros((3, 9, C), jnp.float32) for section_no in range(SECTIONS)]
    point_acc = [jnp.zeros((4, C, C), jnp.float32) for section_no in range(SECTIONS)]
    proj_acc = [jnp.zeros((4 * C, C), jnp.float32) for section_no in range(SECTIONS)]
    head_acc = [jnp.zeros((C, 3), jnp.float32) for section_no in range(SECTIONS)]
    for sample in range(SNAPS):
        label_flat = labels[sample].reshape(pixels, 1)
        onehot = (label_flat == class_ids[None, :]).astype(jnp.float32)
        pixel_weight = jnp.sum(onehot * weight_table[None, :], axis=1)
        current = feats[sample]
        records = []
        for section_no in range(SECTIONS):
            tap_weights = depth_kernel[section_no].astype(jnp.float32)
            plain_in = current.astype(jnp.float32)
            flat_in = current.reshape(pixels, C)
            branch_maps = [depthwise(plain_in, tap_weights[branch], spacings[branch]).astype(jnp.bfloat16) for branch in range(3)]
            pre_acts = [matmul(branch_maps[branch].reshape(pixels, C), point_weight[section_no, branch]) for branch in range(3)]
            pre_acts.append(matmul(flat_in, point_weight[section_no, 3]))
            joined = jnp.concatenate([jnp.maximum(pre_act, 0.0).astype(jnp.bfloat16) for pre_act in pre_acts], axis=1)
            mixed_pre = matmul(joined, proj_weight[section_no])
            result = (flat_in.astype(jnp.float32) + jnp.maximum(mixed_pre, 0.0)).astype(jnp.bfloat16)
            logits = matmul(result, head_weight[section_no])
            chances = jax.nn.softmax(logits, axis=1)
            head_delta = ((factor * pixel_weight)[:, None] * (chances - onehot)).astype(jnp.bfloat16)
            head_acc[section_no] = head_acc[section_no] + outer(result, head_delta)
            from_head = matmul(head_delta, head_weight[section_no].T)
            records.append((tap_weights, plain_in, flat_in, branch_maps, joined, mixed_pre, from_head))
            current = result.reshape(H, COLS, C)
        incoming = jnp.zeros((pixels, C), jnp.float32)
        for section_no in reversed(range(SECTIONS)):
            tap_weights, plain_in, flat_in, branch_maps, joined, mixed_pre, from_head = records[section_no]
            total_grad = from_head + incoming
            gate_mixed = jnp.where(mixed_pre > 0, total_grad, 0.0).astype(jnp.bfloat16)
            proj_acc[section_no] = proj_acc[section_no] + outer(joined, gate_mixed)
            back_joined = matmul(gate_mixed, proj_weight[section_no].T)
            gate_joined = jnp.where(joined > 0, back_joined, 0.0).astype(jnp.bfloat16)
            spread = jnp.zeros((H, COLS, C), jnp.float32)
            point_terms = []
            kernel_terms = []
            for branch in range(3):
                part_grad = gate_joined[:, branch * C:(branch + 1) * C]
                point_terms.append(outer(branch_maps[branch].reshape(pixels, C), part_grad))
                branch_grad = matmul(part_grad, point_weight[section_no, branch].T).astype(jnp.bfloat16)
                back_map, tap_grad = depthwise_back(branch_grad.reshape(H, COLS, C).astype(jnp.float32), plain_in, tap_weights[branch], spacings[branch])
                spread = spread + back_map
                kernel_terms.append(tap_grad)
            part_grad = gate_joined[:, 3 * C:]
            point_terms.append(outer(flat_in, part_grad))
            plain_back = matmul(part_grad, point_weight[section_no, 3].T)
            point_acc[section_no] = point_acc[section_no] + jnp.stack(point_terms)
            kernel_acc[section_no] = kernel_acc[section_no] + jnp.stack(kernel_terms)
            input_grad = (total_grad + plain_back + spread.reshape(pixels, C)).astype(jnp.bfloat16)
            incoming = lax.optimization_barrier(input_grad).astype(jnp.float32)
    return (jnp.stack(kernel_acc), jnp.stack(point_acc), jnp.stack(proj_acc), jnp.stack(head_acc))
```

```python
import jax
import jax.numpy as jnp
from jax import lax
from jax.sharding import PartitionSpec as P

spacings = (12, 24, 36)
loss_scale = 256.0


def recv_from(block, space_by, section_by):
    n_space = lax.axis_size("space")
    n_section = lax.axis_size("section")
    route = []
    for i in range(n_space):
        for s in range(n_section):
            si, ss = i + space_by, s + section_by
            if 0 <= si < n_space and 0 <= ss < n_section:
                route.append((si * n_section + ss, i * n_section + s))
    return lax.ppermute(block, ("space", "section"), route)


def moved(source, offset, axis_dim):
    length = source.shape[axis_dim]
    if abs(offset) >= length:
        return jnp.zeros_like(source)
    widths = [(0, 0)] * source.ndim
    widths[axis_dim] = (max(-offset, 0), max(offset, 0))
    padded = jnp.pad(source, widths)
    begin_at = max(offset, 0)
    return lax.slice_in_dim(padded, begin_at, begin_at + length, axis=axis_dim)


def matmul(first_op, second_op):
    return jnp.dot(first_op, second_op, preferred_element_type=jnp.float32)


def matmul_trans(first_op, second_op):
    return lax.dot_general(
        first_op, second_op, (((1,), (1,)), ((), ())), preferred_element_type=jnp.float32
    )


def outer(first_op, second_op):
    return lax.dot_general(
        first_op, second_op, (((0,), (0,)), ((), ())), preferred_element_type=jnp.float32
    )


def row_views_of(block, section_by):
    views = []
    for spacing in spacings:
        views.append({a: recv_from(block, a * spacing // block.shape[1], section_by) for a in (-1, 1)})
    return views


def forward_block(current, views, weights, label_tile, factor, weight_table):
    taps_all, point_mats, proj_mat, head_mat = weights
    snaps, tile_rows, width_cols, channels = current.shape
    pixels = snaps * tile_rows * width_cols
    plain_in = current.astype(jnp.float32)
    branch_maps = []
    for branch, spacing in enumerate(spacings):
        running = jnp.zeros(current.shape, jnp.float32)
        for row_tap in (-1, 0, 1):
            src = plain_in if row_tap == 0 else views[branch][row_tap].astype(jnp.float32)
            for col_tap in (-1, 0, 1):
                running = running + taps_all[branch, 3 * (row_tap + 1) + col_tap + 1] * moved(
                    src, col_tap * spacing, 2
                )
        branch_maps.append(running.astype(jnp.bfloat16))
    flat_in = current.reshape(pixels, channels)
    pre_acts = [matmul(branch_maps[b].reshape(pixels, channels), point_mats[b]) for b in range(3)]
    pre_acts.append(matmul(flat_in, point_mats[3]))
    joined = jnp.concatenate(
        [jnp.maximum(pre_act, 0.0).astype(jnp.bfloat16) for pre_act in pre_acts], axis=1
    )
    mixed_pre = matmul(joined, proj_mat)
    result = (flat_in.astype(jnp.float32) + jnp.maximum(mixed_pre, 0.0)).astype(jnp.bfloat16)
    logits = matmul(result, head_mat)
    class_ids = jnp.arange(3, dtype=jnp.int32)
    label_flat = label_tile.reshape(pixels, 1)
    onehot = (label_flat == class_ids[None, :]).astype(jnp.float32)
    pixel_weight = jnp.sum(onehot * weight_table[None, :], axis=1)
    chances = jax.nn.softmax(logits, axis=1)
    head_delta = ((factor * pixel_weight)[:, None] * (chances - onehot)).astype(jnp.bfloat16)
    head_term = outer(result, head_delta)
    from_head = matmul_trans(head_delta, head_mat)
    view_list = tuple(views[b][a] for b in range(3) for a in (-1, 1))
    record = (current, view_list, tuple(branch_maps), joined, mixed_pre, from_head)
    return result.reshape(current.shape), head_term, record


def backward_block(record, incoming, weights):
    taps_all, point_mats, proj_mat, head_mat = weights
    current, view_list, branch_maps, joined, mixed_pre, from_head = record
    snaps, tile_rows, width_cols, channels = current.shape
    pixels = snaps * tile_rows * width_cols
    total_grad = from_head + incoming
    gate_mixed = jnp.where(mixed_pre > 0, total_grad, 0.0).astype(jnp.bfloat16)
    proj_term = outer(joined, gate_mixed)
    back_joined = matmul_trans(gate_mixed, proj_mat)
    gate_joined = jnp.where(joined > 0, back_joined, 0.0).astype(jnp.bfloat16)
    flat_in = current.reshape(pixels, channels)
    point_terms = []
    branch_grads = []
    for branch in range(3):
        part_grad = gate_joined[:, branch * channels : (branch + 1) * channels]
        point_terms.append(outer(branch_maps[branch].reshape(pixels, channels), part_grad))
        branch_grads.append(
            matmul_trans(part_grad, point_mats[branch]).astype(jnp.bfloat16).reshape(current.shape)
        )
    part_grad = gate_joined[:, 3 * channels :]
    point_terms.append(outer(flat_in, part_grad))
    plain_back = matmul_trans(part_grad, point_mats[3])
    plain_in = current.astype(jnp.float32)
    local = jnp.zeros(current.shape, jnp.float32)
    kernel_terms = []
    for branch, spacing in enumerate(spacings):
        grad_wide = branch_grads[branch].astype(jnp.float32)
        rows = []
        for row_tap in (-1, 0, 1):
            if row_tap == 0:
                src = plain_in
            else:
                src = view_list[2 * branch + (0 if row_tap < 0 else 1)].astype(jnp.float32)
            for col_tap in (-1, 0, 1):
                partial_sum = jnp.sum(grad_wide * moved(src, col_tap * spacing, 2), axis=(0, 1))
                rows.append(jnp.sum(partial_sum, axis=0))
        for col_tap in (-1, 0, 1):
            local = local + taps_all[branch, 3 + col_tap + 1] * moved(grad_wide, -col_tap * spacing, 2)
        kernel_terms.append(jnp.stack(rows))
    local = total_grad.reshape(current.shape) + plain_back.reshape(current.shape) + local
    return branch_grads, local, (jnp.stack(kernel_terms), jnp.stack(point_terms), proj_term)


def remote_spread(local_in, grads_in, taps_next):
    running = local_in
    for branch, spacing in enumerate(spacings):
        for row_tap in (-1, 1):
            src = grads_in[branch][row_tap].astype(jnp.float32)
            for col_tap in (-1, 0, 1):
                running = running + taps_next[branch, 3 * (row_tap + 1) + col_tap + 1] * moved(
                    src, -col_tap * spacing, 2
                )
    return running


def butterfly_sum(vec, axes, count):
    me = lax.axis_index(axes)
    buf = vec
    steps = count.bit_length() - 1
    for k in range(steps):
        bit = 1 << k
        half = buf.shape[0] // 2
        upper = (me // bit) % 2
        keep = lax.dynamic_slice_in_dim(buf, upper * half, half)
        send = lax.dynamic_slice_in_dim(buf, (1 - upper) * half, half)
        got = lax.ppermute(send, axes, [(i, i ^ bit) for i in range(count)])
        buf = keep + got
    for k in reversed(range(steps)):
        bit = 1 << k
        got = lax.ppermute(buf, axes, [(i, i ^ bit) for i in range(count)])
        upper = (me // bit) % 2
        whole = jnp.zeros((buf.shape[0] * 2,), buf.dtype)
        whole = lax.dynamic_update_slice_in_dim(whole, buf, upper * buf.shape[0], 0)
        buf = lax.dynamic_update_slice_in_dim(whole, got, (1 - upper) * buf.shape[0], 0)
    return buf


def per_device(feats, labels, class_weight, depth_kernel, point_weight, proj_weight, head_weight):
    snaps, tile_rows, width_cols, channels = feats.shape
    space_count = lax.axis_size("space")
    section_count = lax.axis_size("section")
    rep_count = lax.axis_size("rep")
    section_place = lax.axis_index("section")
    factor = loss_scale / (snaps * rep_count * tile_rows * space_count * width_cols)
    weight_table = class_weight.astype(jnp.float32)
    taps_all = depth_kernel[0].astype(jnp.float32)
    weights = (taps_all, point_weight[0], proj_weight[0], head_weight[0])
    taps_next = recv_from(depth_kernel[0], 0, 1).astype(jnp.float32)

    head_grad = jnp.zeros((channels, 3), jnp.float32)
    saved = None
    current = feats
    views = row_views_of(feats, 0)
    for moment in range(section_count):
        is_valid = section_place == moment
        result, head_term, record = forward_block(
            current, views, weights, labels, factor, weight_table
        )
        head_grad = jnp.where(is_valid, head_term, head_grad)
        if saved is None:
            saved = record
        else:
            saved = jax.tree.map(lambda new, old: jnp.where(is_valid, new, old), record, saved)
        if moment < section_count - 1:
            current = recv_from(result, 0, -1)
            views = row_views_of(result, -1)

    kernel_grad = jnp.zeros((3, 9, channels), jnp.float32)
    point_grad = jnp.zeros((4, channels, channels), jnp.float32)
    proj_grad = jnp.zeros((4 * channels, channels), jnp.float32)
    pixels = snaps * tile_rows * width_cols
    incoming = jnp.zeros((pixels, channels), jnp.float32)
    for moment in range(section_count):
        is_valid = section_place == section_count - 1 - moment
        branch_grads, local, terms = backward_block(saved, incoming, weights)
        kernel_grad = jnp.where(is_valid, terms[0], kernel_grad)
        point_grad = jnp.where(is_valid, terms[1], point_grad)
        proj_grad = jnp.where(is_valid, terms[2], proj_grad)
        if moment < section_count - 1:
            local_in = recv_from(local, 0, 1)
            grads_in = [
                {a: recv_from(branch_grads[b], -a * spacings[b] // tile_rows, 1) for a in (-1, 1)}
                for b in range(3)
            ]
            spread = remote_spread(local_in, grads_in, taps_next)
            incoming = spread.astype(jnp.bfloat16).astype(jnp.float32).reshape(pixels, channels)

    parts = (kernel_grad, point_grad, proj_grad, head_grad)
    flat = jnp.concatenate([p.reshape(-1) for p in parts])
    group = space_count * rep_count
    chunk = group * 128
    padded = (flat.shape[0] + chunk - 1) // chunk * chunk
    flat = jnp.pad(flat, (0, padded - flat.shape[0]))
    total = butterfly_sum(flat, ("space", "rep"), group)
    outs = []
    start = 0
    for p in parts:
        outs.append(total[start : start + p.size].reshape((1,) + p.shape))
        start += p.size
    return tuple(outs)


def solution(mesh):
    placed = (
        P("rep", "space", None, None),
        P("rep", "space", None),
        P(),
        P("section", None, None, None),
        P("section", None, None, None),
        P("section", None, None),
        P("section", None, None),
    )
    return jax.shard_map(
        per_device,
        mesh=mesh,
        in_specs=placed,
        out_specs=(
            P("section", None, None, None),
            P("section", None, None, None),
            P("section", None, None),
            P("section", None, None),
        ),
        check_vma=False,
    )
```

```python
import jax
import jax.numpy as jnp
from jax import lax
from jax.sharding import PartitionSpec as P

spacings = (12, 24, 36)
loss_scale = 256.0


def recv_from(block, space_by, section_by):
    n_space = lax.axis_size("space")
    n_section = lax.axis_size("section")
    route = []
    for i in range(n_space):
        for s in range(n_section):
            si, ss = i + space_by, s + section_by
            if 0 <= si < n_space and 0 <= ss < n_section:
                route.append((si * n_section + ss, i * n_section + s))
    return lax.ppermute(block, ("space", "section"), route)


def moved(source, offset, axis_dim):
    length = source.shape[axis_dim]
    if abs(offset) >= length:
        return jnp.zeros_like(source)
    widths = [(0, 0)] * source.ndim
    widths[axis_dim] = (max(-offset, 0), max(offset, 0))
    padded = jnp.pad(source, widths)
    begin_at = max(offset, 0)
    return lax.slice_in_dim(padded, begin_at, begin_at + length, axis=axis_dim)


def matmul(first_op, second_op):
    return jnp.dot(first_op, second_op, preferred_element_type=jnp.float32)


def matmul_trans(first_op, second_op):
    return lax.dot_general(
        first_op, second_op, (((1,), (1,)), ((), ())), preferred_element_type=jnp.float32
    )


def outer(first_op, second_op):
    return lax.dot_general(
        first_op, second_op, (((0,), (0,)), ((), ())), preferred_element_type=jnp.float32
    )


def row_views_of(block, section_by):
    views = []
    for spacing in spacings:
        views.append({a: recv_from(block, a * spacing // block.shape[1], section_by) for a in (-1, 1)})
    return views


def forward_block(current, views, weights, label_tile, factor, weight_table):
    taps_all, point_mats, proj_mat, head_mat = weights
    snaps, tile_rows, width_cols, channels = current.shape
    pixels = snaps * tile_rows * width_cols
    plain_in = current.astype(jnp.float32)
    branch_maps = []
    for branch, spacing in enumerate(spacings):
        running = jnp.zeros(current.shape, jnp.float32)
        for row_tap in (-1, 0, 1):
            src = plain_in if row_tap == 0 else views[branch][row_tap].astype(jnp.float32)
            for col_tap in (-1, 0, 1):
                running = running + taps_all[branch, 3 * (row_tap + 1) + col_tap + 1] * moved(
                    src, col_tap * spacing, 2
                )
        branch_maps.append(running.astype(jnp.bfloat16))
    flat_in = current.reshape(pixels, channels)
    pre_acts = [matmul(branch_maps[b].reshape(pixels, channels), point_mats[b]) for b in range(3)]
    pre_acts.append(matmul(flat_in, point_mats[3]))
    joined = jnp.concatenate(
        [jnp.maximum(pre_act, 0.0).astype(jnp.bfloat16) for pre_act in pre_acts], axis=1
    )
    mixed_pre = matmul(joined, proj_mat)
    result = (flat_in.astype(jnp.float32) + jnp.maximum(mixed_pre, 0.0)).astype(jnp.bfloat16)
    logits = matmul(result, head_mat)
    class_ids = jnp.arange(3, dtype=jnp.int32)
    label_flat = label_tile.reshape(pixels, 1)
    onehot = (label_flat == class_ids[None, :]).astype(jnp.float32)
    pixel_weight = jnp.sum(onehot * weight_table[None, :], axis=1)
    chances = jax.nn.softmax(logits, axis=1)
    head_delta = ((factor * pixel_weight)[:, None] * (chances - onehot)).astype(jnp.bfloat16)
    head_term = outer(result, head_delta)
    from_head = matmul_trans(head_delta, head_mat)
    view_list = tuple(views[b][a] for b in range(3) for a in (-1, 1))
    record = (current, view_list, tuple(branch_maps), joined, mixed_pre, from_head)
    return result.reshape(current.shape), head_term, record


def backward_block(record, incoming, weights):
    taps_all, point_mats, proj_mat, head_mat = weights
    current, view_list, branch_maps, joined, mixed_pre, from_head = record
    snaps, tile_rows, width_cols, channels = current.shape
    pixels = snaps * tile_rows * width_cols
    total_grad = from_head + incoming
    gate_mixed = jnp.where(mixed_pre > 0, total_grad, 0.0).astype(jnp.bfloat16)
    proj_term = outer(joined, gate_mixed)
    back_joined = matmul_trans(gate_mixed, proj_mat)
    gate_joined = jnp.where(joined > 0, back_joined, 0.0).astype(jnp.bfloat16)
    flat_in = current.reshape(pixels, channels)
    point_terms = []
    branch_grads = []
    for branch in range(3):
        part_grad = gate_joined[:, branch * channels : (branch + 1) * channels]
        point_terms.append(outer(branch_maps[branch].reshape(pixels, channels), part_grad))
        branch_grads.append(
            matmul_trans(part_grad, point_mats[branch]).astype(jnp.bfloat16).reshape(current.shape)
        )
    part_grad = gate_joined[:, 3 * channels :]
    point_terms.append(outer(flat_in, part_grad))
    plain_back = matmul_trans(part_grad, point_mats[3])
    plain_in = current.astype(jnp.float32)
    local = jnp.zeros(current.shape, jnp.float32)
    kernel_terms = []
    for branch, spacing in enumerate(spacings):
        grad_wide = branch_grads[branch].astype(jnp.float32)
        rows = []
        for row_tap in (-1, 0, 1):
            if row_tap == 0:
                src = plain_in
            else:
                src = view_list[2 * branch + (0 if row_tap < 0 else 1)].astype(jnp.float32)
            for col_tap in (-1, 0, 1):
                partial_sum = jnp.sum(grad_wide * moved(src, col_tap * spacing, 2), axis=(0, 1))
                rows.append(jnp.sum(partial_sum, axis=0))
        for col_tap in (-1, 0, 1):
            local = local + taps_all[branch, 3 + col_tap + 1] * moved(grad_wide, -col_tap * spacing, 2)
        kernel_terms.append(jnp.stack(rows))
    local = total_grad.reshape(current.shape) + plain_back.reshape(current.shape) + local
    return branch_grads, local, (jnp.stack(kernel_terms), jnp.stack(point_terms), proj_term)


def remote_spread(local_in, grads_in, taps_next):
    running = local_in
    for branch, spacing in enumerate(spacings):
        for row_tap in (-1, 1):
            src = grads_in[branch][row_tap].astype(jnp.float32)
            for col_tap in (-1, 0, 1):
                running = running + taps_next[branch, 3 * (row_tap + 1) + col_tap + 1] * moved(
                    src, -col_tap * spacing, 2
                )
    return running


def butterfly_sum(vec, axes, count):
    me = lax.axis_index(axes)
    buf = vec
    steps = count.bit_length() - 1
    for k in range(steps):
        bit = 1 << k
        half = buf.shape[0] // 2
        upper = (me // bit) % 2
        keep = lax.dynamic_slice_in_dim(buf, upper * half, half)
        send = lax.dynamic_slice_in_dim(buf, (1 - upper) * half, half)
        got = lax.ppermute(send, axes, [(i, i ^ bit) for i in range(count)])
        buf = keep + got
    for k in reversed(range(steps)):
        bit = 1 << k
        got = lax.ppermute(buf, axes, [(i, i ^ bit) for i in range(count)])
        upper = (me // bit) % 2 == 1
        buf = jnp.where(upper, jnp.concatenate([got, buf]), jnp.concatenate([buf, got]))
    return buf


def per_device(feats, labels, class_weight, depth_kernel, point_weight, proj_weight, head_weight):
    snaps, tile_rows, width_cols, channels = feats.shape
    space_count = lax.axis_size("space")
    section_count = lax.axis_size("section")
    rep_count = lax.axis_size("rep")
    section_place = lax.axis_index("section")
    factor = loss_scale / (snaps * rep_count * tile_rows * space_count * width_cols)
    weight_table = class_weight.astype(jnp.float32)
    taps_all = depth_kernel[0].astype(jnp.float32)
    weights = (taps_all, point_weight[0], proj_weight[0], head_weight[0])
    taps_next = recv_from(depth_kernel[0], 0, 1).astype(jnp.float32)

    head_grad = jnp.zeros((channels, 3), jnp.float32)
    saved = None
    current = feats
    views = row_views_of(feats, 0)
    for moment in range(section_count):
        is_valid = section_place == moment
        result, head_term, record = forward_block(
            current, views, weights, labels, factor, weight_table
        )
        head_grad = jnp.where(is_valid, head_term, head_grad)
        if saved is None:
            saved = record
        else:
            saved = jax.tree.map(lambda new, old: jnp.where(is_valid, new, old), record, saved)
        if moment < section_count - 1:
            current = recv_from(result, 0, -1)
            views = row_views_of(result, -1)

    kernel_grad = jnp.zeros((3, 9, channels), jnp.float32)
    point_grad = jnp.zeros((4, channels, channels), jnp.float32)
    proj_grad = jnp.zeros((4 * channels, channels), jnp.float32)
    pixels = snaps * tile_rows * width_cols
    incoming = jnp.zeros((pixels, channels), jnp.float32)
    for moment in range(section_count):
        is_valid = section_place == section_count - 1 - moment
        branch_grads, local, terms = backward_block(saved, incoming, weights)
        kernel_grad = jnp.where(is_valid, terms[0], kernel_grad)
        point_grad = jnp.where(is_valid, terms[1], point_grad)
        proj_grad = jnp.where(is_valid, terms[2], proj_grad)
        if moment < section_count - 1:
            local_in = recv_from(local, 0, 1)
            grads_in = [
                {a: recv_from(branch_grads[b], -a * spacings[b] // tile_rows, 1) for a in (-1, 1)}
                for b in range(3)
            ]
            spread = remote_spread(local_in, grads_in, taps_next)
            incoming = spread.astype(jnp.bfloat16).astype(jnp.float32).reshape(pixels, channels)

    parts = (kernel_grad, point_grad, proj_grad, head_grad)
    flat = jnp.concatenate([p.reshape(-1) for p in parts])
    group = space_count * rep_count
    chunk = group * 128
    padded = (flat.shape[0] + chunk - 1) // chunk * chunk
    flat = jnp.pad(flat, (0, padded - flat.shape[0]))
    total = butterfly_sum(flat, ("space", "rep"), group)
    outs = []
    start = 0
    for p in parts:
        outs.append(total[start : start + p.size].reshape((1,) + p.shape))
        start += p.size
    return tuple(outs)


def solution(mesh):
    placed = (
        P("rep", "space", None, None),
        P("rep", "space", None),
        P(),
        P("section", None, None, None),
        P("section", None, None, None),
        P("section", None, None),
        P("section", None, None),
    )
    return jax.shard_map(
        per_device,
        mesh=mesh,
        in_specs=placed,
        out_specs=(
            P("section", None, None, None),
            P("section", None, None, None),
            P("section", None, None),
            P("section", None, None),
        ),
        check_vma=False,
    )
```

```python
import jax
import jax.numpy as jnp
from jax import lax
from jax.sharding import PartitionSpec as P

spacings = (12, 24, 36)
loss_scale = 256.0


def recv_from(block, space_by, section_by):
    n_space = lax.axis_size("space")
    n_section = lax.axis_size("section")
    route = []
    for i in range(n_space):
        for s in range(n_section):
            si, ss = i + space_by, s + section_by
            if 0 <= si < n_space and 0 <= ss < n_section:
                route.append((si * n_section + ss, i * n_section + s))
    return lax.ppermute(block, ("space", "section"), route)


def moved(source, offset, axis_dim):
    length = source.shape[axis_dim]
    if abs(offset) >= length:
        return jnp.zeros_like(source)
    widths = [(0, 0)] * source.ndim
    widths[axis_dim] = (max(-offset, 0), max(offset, 0))
    padded = jnp.pad(source, widths)
    begin_at = max(offset, 0)
    return lax.slice_in_dim(padded, begin_at, begin_at + length, axis=axis_dim)


def matmul(first_op, second_op):
    return jnp.dot(first_op, second_op, preferred_element_type=jnp.float32)


def matmul_trans(first_op, second_op):
    return lax.dot_general(
        first_op, second_op, (((1,), (1,)), ((), ())), preferred_element_type=jnp.float32
    )


def outer(first_op, second_op):
    return lax.dot_general(
        first_op, second_op, (((0,), (0,)), ((), ())), preferred_element_type=jnp.float32
    )


def row_views_of(block, section_by):
    views = []
    for spacing in spacings:
        views.append({a: recv_from(block, a * spacing // block.shape[1], section_by) for a in (-1, 1)})
    return views


def forward_block(current, views, weights, label_tile, factor, weight_table):
    taps_all, point_mats, proj_mat, head_mat = weights
    snaps, tile_rows, width_cols, channels = current.shape
    pixels = snaps * tile_rows * width_cols
    plain_in = current.astype(jnp.float32)
    branch_maps = []
    for branch, spacing in enumerate(spacings):
        running = jnp.zeros(current.shape, jnp.float32)
        for row_tap in (-1, 0, 1):
            src = plain_in if row_tap == 0 else views[branch][row_tap].astype(jnp.float32)
            for col_tap in (-1, 0, 1):
                running = running + taps_all[branch, 3 * (row_tap + 1) + col_tap + 1] * moved(
                    src, col_tap * spacing, 2
                )
        branch_maps.append(running.astype(jnp.bfloat16))
    flat_in = current.reshape(pixels, channels)
    pre_acts = [matmul(branch_maps[b].reshape(pixels, channels), point_mats[b]) for b in range(3)]
    pre_acts.append(matmul(flat_in, point_mats[3]))
    joined = jnp.concatenate(
        [jnp.maximum(pre_act, 0.0).astype(jnp.bfloat16) for pre_act in pre_acts], axis=1
    )
    mixed_pre = matmul(joined, proj_mat)
    result = (flat_in.astype(jnp.float32) + jnp.maximum(mixed_pre, 0.0)).astype(jnp.bfloat16)
    logits = matmul(result, head_mat)
    class_ids = jnp.arange(3, dtype=jnp.int32)
    label_flat = label_tile.reshape(pixels, 1)
    onehot = (label_flat == class_ids[None, :]).astype(jnp.float32)
    pixel_weight = jnp.sum(onehot * weight_table[None, :], axis=1)
    chances = jax.nn.softmax(logits, axis=1)
    head_delta = ((factor * pixel_weight)[:, None] * (chances - onehot)).astype(jnp.bfloat16)
    head_term = outer(result, head_delta)
    from_head = matmul_trans(head_delta, head_mat)
    view_list = tuple(views[b][a] for b in range(3) for a in (-1, 1))
    record = (current, view_list, tuple(branch_maps), joined, mixed_pre, from_head)
    return result.reshape(current.shape), head_term, record


def backward_block(record, incoming, weights):
    taps_all, point_mats, proj_mat, head_mat = weights
    current, view_list, branch_maps, joined, mixed_pre, from_head = record
    snaps, tile_rows, width_cols, channels = current.shape
    pixels = snaps * tile_rows * width_cols
    total_grad = from_head + incoming
    gate_mixed = jnp.where(mixed_pre > 0, total_grad, 0.0).astype(jnp.bfloat16)
    proj_term = outer(joined, gate_mixed)
    back_joined = matmul_trans(gate_mixed, proj_mat)
    gate_joined = jnp.where(joined > 0, back_joined, 0.0).astype(jnp.bfloat16)
    flat_in = current.reshape(pixels, channels)
    point_terms = []
    branch_grads = []
    for branch in range(3):
        part_grad = gate_joined[:, branch * channels : (branch + 1) * channels]
        point_terms.append(outer(branch_maps[branch].reshape(pixels, channels), part_grad))
        branch_grads.append(
            matmul_trans(part_grad, point_mats[branch]).astype(jnp.bfloat16).reshape(current.shape)
        )
    part_grad = gate_joined[:, 3 * channels :]
    point_terms.append(outer(flat_in, part_grad))
    plain_back = matmul_trans(part_grad, point_mats[3])
    plain_in = current.astype(jnp.float32)
    local = jnp.zeros(current.shape, jnp.float32)
    kernel_terms = []
    for branch, spacing in enumerate(spacings):
        grad_wide = branch_grads[branch].astype(jnp.float32)
        rows = []
        for row_tap in (-1, 0, 1):
            if row_tap == 0:
                src = plain_in
            else:
                src = view_list[2 * branch + (0 if row_tap < 0 else 1)].astype(jnp.float32)
            for col_tap in (-1, 0, 1):
                partial_sum = jnp.sum(grad_wide * moved(src, col_tap * spacing, 2), axis=(0, 1))
                rows.append(jnp.sum(partial_sum, axis=0))
        for col_tap in (-1, 0, 1):
            local = local + taps_all[branch, 3 + col_tap + 1] * moved(grad_wide, -col_tap * spacing, 2)
        kernel_terms.append(jnp.stack(rows))
    local = total_grad.reshape(current.shape) + plain_back.reshape(current.shape) + local
    return branch_grads, local, (jnp.stack(kernel_terms), jnp.stack(point_terms), proj_term)


def remote_spread(local_in, grads_in, taps_next):
    running = local_in
    for branch, spacing in enumerate(spacings):
        for row_tap in (-1, 1):
            src = grads_in[branch][row_tap].astype(jnp.float32)
            for col_tap in (-1, 0, 1):
                running = running + taps_next[branch, 3 * (row_tap + 1) + col_tap + 1] * moved(
                    src, -col_tap * spacing, 2
                )
    return running


def radices_of(count):
    radices = []
    while count % 4 == 0:
        radices.append(4)
        count //= 4
    while count % 2 == 0:
        radices.append(2)
        count //= 2
    return radices


def digit_route(count, weight, radix, offset):
    route = []
    for i in range(count):
        digit = (i // weight) % radix
        target = (digit + offset) % radix
        route.append((i, i + (target - digit) * weight))
    return route


def tree_sum(block, axes, count):
    me = lax.axis_index(axes)
    radices = radices_of(count)
    weights = []
    weight = 1
    for radix in radices:
        weights.append(weight)
        weight *= radix
    buf = block
    for radix, weight in zip(radices, weights):
        piece = buf.shape[0] // radix
        digit = (me // weight) % radix
        total = lax.dynamic_slice_in_dim(buf, digit * piece, piece, 0)
        for offset in range(1, radix):
            send = lax.dynamic_slice_in_dim(buf, ((digit + offset) % radix) * piece, piece, 0)
            total = total + lax.ppermute(send, axes, digit_route(count, weight, radix, offset))
        buf = total
    for radix, weight in reversed(list(zip(radices, weights))):
        digit = (me // weight) % radix
        got = [buf] + [
            lax.ppermute(buf, axes, digit_route(count, weight, radix, offset))
            for offset in range(1, radix)
        ]
        blocks = []
        for place in range(radix):
            which = (digit - place) % radix
            chosen = got[0]
            for offset in range(1, radix):
                chosen = jnp.where(which == offset, got[offset], chosen)
            blocks.append(chosen)
        buf = jnp.concatenate(blocks, axis=0)
    return buf


def per_device(feats, labels, class_weight, depth_kernel, point_weight, proj_weight, head_weight):
    snaps, tile_rows, width_cols, channels = feats.shape
    space_count = lax.axis_size("space")
    section_count = lax.axis_size("section")
    rep_count = lax.axis_size("rep")
    section_place = lax.axis_index("section")
    factor = loss_scale / (snaps * rep_count * tile_rows * space_count * width_cols)
    weight_table = class_weight.astype(jnp.float32)
    taps_all = depth_kernel[0].astype(jnp.float32)
    weights = (taps_all, point_weight[0], proj_weight[0], head_weight[0])
    taps_next = recv_from(depth_kernel[0], 0, 1).astype(jnp.float32)

    head_grad = jnp.zeros((channels, 3), jnp.float32)
    saved = None
    current = feats
    views = row_views_of(feats, 0)
    for moment in range(section_count):
        is_valid = section_place == moment
        result, head_term, record = forward_block(
            current, views, weights, labels, factor, weight_table
        )
        head_grad = jnp.where(is_valid, head_term, head_grad)
        if saved is None:
            saved = record
        else:
            saved = jax.tree.map(lambda new, old: jnp.where(is_valid, new, old), record, saved)
        if moment < section_count - 1:
            current = recv_from(result, 0, -1)
            views = row_views_of(result, -1)

    kernel_grad = jnp.zeros((3, 9, channels), jnp.float32)
    point_grad = jnp.zeros((4, channels, channels), jnp.float32)
    proj_grad = jnp.zeros((4 * channels, channels), jnp.float32)
    pixels = snaps * tile_rows * width_cols
    incoming = jnp.zeros((pixels, channels), jnp.float32)
    for moment in range(section_count):
        is_valid = section_place == section_count - 1 - moment
        branch_grads, local, terms = backward_block(saved, incoming, weights)
        kernel_grad = jnp.where(is_valid, terms[0], kernel_grad)
        point_grad = jnp.where(is_valid, terms[1], point_grad)
        proj_grad = jnp.where(is_valid, terms[2], proj_grad)
        if moment < section_count - 1:
            local_in = recv_from(local, 0, 1)
            grads_in = [
                {a: recv_from(branch_grads[b], -a * spacings[b] // tile_rows, 1) for a in (-1, 1)}
                for b in range(3)
            ]
            spread = remote_spread(local_in, grads_in, taps_next)
            incoming = spread.astype(jnp.bfloat16).astype(jnp.float32).reshape(pixels, channels)

    parts = (kernel_grad, point_grad, proj_grad, head_grad)
    rows = [p.reshape(-1, channels) for p in parts]
    flat = jnp.concatenate(rows, axis=0)
    group = space_count * rep_count
    chunk = group * 8
    padded = (flat.shape[0] + chunk - 1) // chunk * chunk
    flat = jnp.pad(flat, ((0, padded - flat.shape[0]), (0, 0)))
    total = tree_sum(flat, ("space", "rep"), group)
    outs = []
    start = 0
    for p, r in zip(parts, rows):
        outs.append(total[start : start + r.shape[0]].reshape((1,) + p.shape))
        start += r.shape[0]
    return tuple(outs)


def solution(mesh):
    placed = (
        P("rep", "space", None, None),
        P("rep", "space", None),
        P(),
        P("section", None, None, None),
        P("section", None, None, None),
        P("section", None, None),
        P("section", None, None),
    )
    return jax.shard_map(
        per_device,
        mesh=mesh,
        in_specs=placed,
        out_specs=(
            P("section", None, None, None),
            P("section", None, None, None),
            P("section", None, None),
            P("section", None, None),
        ),
        check_vma=False,
    )
```

```python
import jax
import jax.numpy as jnp
from jax import lax
from jax.sharding import PartitionSpec as P

spacings = (12, 24, 36)
loss_scale = 256.0


def recv_from(block, space_by, section_by):
    n_space = lax.axis_size("space")
    n_section = lax.axis_size("section")
    route = []
    for i in range(n_space):
        for s in range(n_section):
            si, ss = i + space_by, s + section_by
            if 0 <= si < n_space and 0 <= ss < n_section:
                route.append((si * n_section + ss, i * n_section + s))
    return lax.ppermute(block, ("space", "section"), route)


def moved(source, offset, axis_dim):
    length = source.shape[axis_dim]
    if abs(offset) >= length:
        return jnp.zeros_like(source)
    widths = [(0, 0)] * source.ndim
    widths[axis_dim] = (max(-offset, 0), max(offset, 0))
    padded = jnp.pad(source, widths)
    begin_at = max(offset, 0)
    return lax.slice_in_dim(padded, begin_at, begin_at + length, axis=axis_dim)


def matmul(first_op, second_op):
    return jnp.dot(first_op, second_op, preferred_element_type=jnp.float32)


def matmul_trans(first_op, second_op):
    return lax.dot_general(
        first_op, second_op, (((1,), (1,)), ((), ())), preferred_element_type=jnp.float32
    )


def outer(first_op, second_op):
    return lax.dot_general(
        first_op, second_op, (((0,), (0,)), ((), ())), preferred_element_type=jnp.float32
    )


def row_views_of(block, step):
    return [{a: moved(block, a * spacing // step, 1) for a in (-1, 1)} for spacing in spacings]


def forward_block(current, views, weights, label_tile, factor, weight_table, step):
    taps_all, point_mats, proj_mat, head_mat = weights
    snaps, tile_rows, width_cols, channels = current.shape
    pixels = snaps * tile_rows * width_cols
    plain_in = current.astype(jnp.float32)
    branch_maps = []
    for branch, spacing in enumerate(spacings):
        running = jnp.zeros(current.shape, jnp.float32)
        for row_tap in (-1, 0, 1):
            src = plain_in if row_tap == 0 else views[branch][row_tap].astype(jnp.float32)
            for col_tap in (-1, 0, 1):
                running = running + taps_all[branch, 3 * (row_tap + 1) + col_tap + 1] * moved(
                    src, col_tap * spacing // step, 2
                )
        branch_maps.append(running.astype(jnp.bfloat16))
    flat_in = current.reshape(pixels, channels)
    pre_acts = [matmul(branch_maps[b].reshape(pixels, channels), point_mats[b]) for b in range(3)]
    pre_acts.append(matmul(flat_in, point_mats[3]))
    joined = jnp.concatenate(
        [jnp.maximum(pre_act, 0.0).astype(jnp.bfloat16) for pre_act in pre_acts], axis=1
    )
    mixed_pre = matmul(joined, proj_mat)
    result = (flat_in.astype(jnp.float32) + jnp.maximum(mixed_pre, 0.0)).astype(jnp.bfloat16)
    logits = matmul(result, head_mat)
    class_ids = jnp.arange(3, dtype=jnp.int32)
    label_flat = label_tile.reshape(pixels, 1)
    onehot = (label_flat == class_ids[None, :]).astype(jnp.float32)
    pixel_weight = jnp.sum(onehot * weight_table[None, :], axis=1)
    chances = jax.nn.softmax(logits, axis=1)
    head_delta = ((factor * pixel_weight)[:, None] * (chances - onehot)).astype(jnp.bfloat16)
    head_term = outer(result, head_delta)
    from_head = matmul_trans(head_delta, head_mat)
    view_list = tuple(views[b][a] for b in range(3) for a in (-1, 1))
    record = (current, view_list, tuple(branch_maps), joined, mixed_pre, from_head)
    return result.reshape(current.shape), head_term, record


def backward_block(record, incoming, weights, step):
    taps_all, point_mats, proj_mat, head_mat = weights
    current, view_list, branch_maps, joined, mixed_pre, from_head = record
    snaps, tile_rows, width_cols, channels = current.shape
    pixels = snaps * tile_rows * width_cols
    total_grad = from_head + incoming
    gate_mixed = jnp.where(mixed_pre > 0, total_grad, 0.0).astype(jnp.bfloat16)
    proj_term = outer(joined, gate_mixed)
    back_joined = matmul_trans(gate_mixed, proj_mat)
    gate_joined = jnp.where(joined > 0, back_joined, 0.0).astype(jnp.bfloat16)
    flat_in = current.reshape(pixels, channels)
    point_terms = []
    branch_grads = []
    for branch in range(3):
        part_grad = gate_joined[:, branch * channels : (branch + 1) * channels]
        point_terms.append(outer(branch_maps[branch].reshape(pixels, channels), part_grad))
        branch_grads.append(
            matmul_trans(part_grad, point_mats[branch]).astype(jnp.bfloat16).reshape(current.shape)
        )
    part_grad = gate_joined[:, 3 * channels :]
    point_terms.append(outer(flat_in, part_grad))
    plain_back = matmul_trans(part_grad, point_mats[3])
    plain_in = current.astype(jnp.float32)
    local = jnp.zeros(current.shape, jnp.float32)
    kernel_terms = []
    for branch, spacing in enumerate(spacings):
        grad_wide = branch_grads[branch].astype(jnp.float32)
        rows = []
        for row_tap in (-1, 0, 1):
            if row_tap == 0:
                src = plain_in
            else:
                src = view_list[2 * branch + (0 if row_tap < 0 else 1)].astype(jnp.float32)
            for col_tap in (-1, 0, 1):
                partial_sum = jnp.sum(grad_wide * moved(src, col_tap * spacing // step, 2), axis=(0, 1))
                rows.append(jnp.sum(partial_sum, axis=0))
        for row_tap in (-1, 0, 1):
            row_moved = moved(grad_wide, -row_tap * spacing // step, 1)
            for col_tap in (-1, 0, 1):
                local = local + taps_all[branch, 3 * (row_tap + 1) + col_tap + 1] * moved(
                    row_moved, -col_tap * spacing // step, 2
                )
        kernel_terms.append(jnp.stack(rows))
    local = total_grad.reshape(current.shape) + plain_back.reshape(current.shape) + local
    return branch_grads, local, (jnp.stack(kernel_terms), jnp.stack(point_terms), proj_term)


def butterfly_sum(vec, axes, count):
    me = lax.axis_index(axes)
    buf = vec
    steps = count.bit_length() - 1
    for k in range(steps):
        bit = 1 << k
        half = buf.shape[0] // 2
        upper = (me // bit) % 2
        keep = lax.dynamic_slice_in_dim(buf, upper * half, half)
        send = lax.dynamic_slice_in_dim(buf, (1 - upper) * half, half)
        got = lax.ppermute(send, axes, [(i, i ^ bit) for i in range(count)])
        buf = keep + got
    for k in reversed(range(steps)):
        bit = 1 << k
        got = lax.ppermute(buf, axes, [(i, i ^ bit) for i in range(count)])
        upper = (me // bit) % 2 == 1
        buf = jnp.where(upper, jnp.concatenate([got, buf]), jnp.concatenate([buf, got]))
    return buf


def to_classes(block, step, space_count):
    snaps, rows, cols = block.shape[:3]
    rest = block.shape[3:]
    split = block.reshape((snaps, rows, cols // step, step) + rest)
    order = (0, 1, 3, 2) + tuple(range(4, split.ndim))
    send = split.transpose(order).reshape((space_count, cols // step) + rest)
    got = lax.all_to_all(send, "space", 0, 0, tiled=True)
    return got[None]


def per_device(feats, labels, class_weight, depth_kernel, point_weight, proj_weight, head_weight):
    snaps, tile_rows, width_cols, channels = feats.shape
    space_count = lax.axis_size("space")
    section_count = lax.axis_size("section")
    rep_count = lax.axis_size("rep")
    section_place = lax.axis_index("section")
    factor = loss_scale / (snaps * rep_count * tile_rows * space_count * width_cols)
    weight_table = class_weight.astype(jnp.float32)
    taps_all = depth_kernel[0].astype(jnp.float32)
    weights = (taps_all, point_weight[0], proj_weight[0], head_weight[0])
    step = tile_rows
    assert snaps * tile_rows * step == space_count and width_cols % step == 0
    assert all(spacing % step == 0 for spacing in spacings)
    start_map = to_classes(feats, step, space_count)
    label_map = to_classes(labels, step, space_count)

    head_grad = jnp.zeros((channels, 3), jnp.float32)
    saved = None
    current = start_map
    for moment in range(section_count):
        is_valid = section_place == moment
        views = row_views_of(current, step)
        result, head_term, record = forward_block(
            current, views, weights, label_map, factor, weight_table, step
        )
        head_grad = jnp.where(is_valid, head_term, head_grad)
        if saved is None:
            saved = record
        else:
            saved = jax.tree.map(lambda new, old: jnp.where(is_valid, new, old), record, saved)
        if moment < section_count - 1:
            current = recv_from(result, 0, -1)

    kernel_grad = jnp.zeros((3, 9, channels), jnp.float32)
    point_grad = jnp.zeros((4, channels, channels), jnp.float32)
    proj_grad = jnp.zeros((4 * channels, channels), jnp.float32)
    pixels = start_map.size // channels
    incoming = jnp.zeros((pixels, channels), jnp.float32)
    for moment in range(section_count):
        is_valid = section_place == section_count - 1 - moment
        branch_grads, local, terms = backward_block(saved, incoming, weights, step)
        kernel_grad = jnp.where(is_valid, terms[0], kernel_grad)
        point_grad = jnp.where(is_valid, terms[1], point_grad)
        proj_grad = jnp.where(is_valid, terms[2], proj_grad)
        if moment < section_count - 1:
            arriving = recv_from(local.astype(jnp.bfloat16), 0, 1)
            incoming = arriving.astype(jnp.float32).reshape(pixels, channels)

    parts = (kernel_grad, point_grad, proj_grad, head_grad)
    flat = jnp.concatenate([p.reshape(-1) for p in parts])
    group = space_count * rep_count
    chunk = group * 128
    padded = (flat.shape[0] + chunk - 1) // chunk * chunk
    flat = jnp.pad(flat, (0, padded - flat.shape[0]))
    total = butterfly_sum(flat, ("space", "rep"), group)
    outs = []
    start = 0
    for p in parts:
        outs.append(total[start : start + p.size].reshape((1,) + p.shape))
        start += p.size
    return tuple(outs)


def solution(mesh):
    placed = (
        P("rep", "space", None, None),
        P("rep", "space", None),
        P(),
        P("section", None, None, None),
        P("section", None, None, None),
        P("section", None, None),
        P("section", None, None),
    )
    return jax.shard_map(
        per_device,
        mesh=mesh,
        in_specs=placed,
        out_specs=(
            P("section", None, None, None),
            P("section", None, None, None),
            P("section", None, None),
            P("section", None, None),
        ),
        check_vma=False,
    )
```

```python
import jax
import jax.numpy as jnp
from jax import lax
from jax.sharding import PartitionSpec as P

spacings = (12, 24, 36)
loss_scale = 256.0


def recv_from(block, space_by, section_by):
    n_space = lax.axis_size("space")
    n_section = lax.axis_size("section")
    route = []
    for i in range(n_space):
        for s in range(n_section):
            si, ss = i + space_by, s + section_by
            if 0 <= si < n_space and 0 <= ss < n_section:
                route.append((si * n_section + ss, i * n_section + s))
    return lax.ppermute(block, ("space", "section"), route)


def moved(source, offset, axis_dim):
    length = source.shape[axis_dim]
    if abs(offset) >= length:
        return jnp.zeros_like(source)
    widths = [(0, 0)] * source.ndim
    widths[axis_dim] = (max(-offset, 0), max(offset, 0))
    padded = jnp.pad(source, widths)
    begin_at = max(offset, 0)
    return lax.slice_in_dim(padded, begin_at, begin_at + length, axis=axis_dim)


def matmul(first_op, second_op):
    return jnp.dot(first_op, second_op, preferred_element_type=jnp.float32)


def matmul_trans(first_op, second_op):
    return lax.dot_general(
        first_op, second_op, (((1,), (1,)), ((), ())), preferred_element_type=jnp.float32
    )


def outer(first_op, second_op):
    return lax.dot_general(
        first_op, second_op, (((0,), (0,)), ((), ())), preferred_element_type=jnp.float32
    )


def row_views_of(block, step):
    return [{a: moved(block, a * spacing // step, 2) for a in (-1, 1)} for spacing in spacings]


def forward_block(current, views, weights, label_tile, factor, weight_table, step):
    taps_all, point_mats, proj_mat, head_mat = weights
    snaps, tile_rows, width_cols, channels = current.shape
    pixels = snaps * tile_rows * width_cols
    plain_in = current.astype(jnp.float32)
    branch_maps = []
    for branch, spacing in enumerate(spacings):
        running = jnp.zeros(current.shape, jnp.float32)
        for row_tap in (-1, 0, 1):
            src = plain_in if row_tap == 0 else views[branch][row_tap].astype(jnp.float32)
            for col_tap in (-1, 0, 1):
                running = running + taps_all[branch, 3 * (row_tap + 1) + col_tap + 1] * moved(
                    src, col_tap * spacing // step, 1
                )
        branch_maps.append(running.astype(jnp.bfloat16))
    flat_in = current.reshape(pixels, channels)
    pre_acts = [matmul(branch_maps[b].reshape(pixels, channels), point_mats[b]) for b in range(3)]
    pre_acts.append(matmul(flat_in, point_mats[3]))
    joined = jnp.concatenate(
        [jnp.maximum(pre_act, 0.0).astype(jnp.bfloat16) for pre_act in pre_acts], axis=1
    )
    mixed_pre = matmul(joined, proj_mat)
    result = (flat_in.astype(jnp.float32) + jnp.maximum(mixed_pre, 0.0)).astype(jnp.bfloat16)
    logits = matmul(result, head_mat)
    class_ids = jnp.arange(3, dtype=jnp.int32)
    label_flat = label_tile.reshape(pixels, 1)
    onehot = (label_flat == class_ids[None, :]).astype(jnp.float32)
    pixel_weight = jnp.sum(onehot * weight_table[None, :], axis=1)
    chances = jax.nn.softmax(logits, axis=1)
    head_delta = ((factor * pixel_weight)[:, None] * (chances - onehot)).astype(jnp.bfloat16)
    head_term = outer(result, head_delta)
    from_head = matmul_trans(head_delta, head_mat)
    view_list = tuple(views[b][a] for b in range(3) for a in (-1, 1))
    record = (current, view_list, tuple(branch_maps), joined, mixed_pre, from_head)
    return result.reshape(current.shape), head_term, record


def backward_block(record, incoming, weights, step):
    taps_all, point_mats, proj_mat, head_mat = weights
    current, view_list, branch_maps, joined, mixed_pre, from_head = record
    snaps, tile_rows, width_cols, channels = current.shape
    pixels = snaps * tile_rows * width_cols
    total_grad = from_head + incoming
    gate_mixed = jnp.where(mixed_pre > 0, total_grad, 0.0).astype(jnp.bfloat16)
    proj_term = outer(joined, gate_mixed)
    back_joined = matmul_trans(gate_mixed, proj_mat)
    gate_joined = jnp.where(joined > 0, back_joined, 0.0).astype(jnp.bfloat16)
    flat_in = current.reshape(pixels, channels)
    point_terms = []
    branch_grads = []
    for branch in range(3):
        part_grad = gate_joined[:, branch * channels : (branch + 1) * channels]
        point_terms.append(outer(branch_maps[branch].reshape(pixels, channels), part_grad))
        branch_grads.append(
            matmul_trans(part_grad, point_mats[branch]).astype(jnp.bfloat16).reshape(current.shape)
        )
    part_grad = gate_joined[:, 3 * channels :]
    point_terms.append(outer(flat_in, part_grad))
    plain_back = matmul_trans(part_grad, point_mats[3])
    plain_in = current.astype(jnp.float32)
    local = jnp.zeros(current.shape, jnp.float32)
    kernel_terms = []
    for branch, spacing in enumerate(spacings):
        grad_wide = branch_grads[branch].astype(jnp.float32)
        rows = []
        for row_tap in (-1, 0, 1):
            if row_tap == 0:
                src = plain_in
            else:
                src = view_list[2 * branch + (0 if row_tap < 0 else 1)].astype(jnp.float32)
            for col_tap in (-1, 0, 1):
                partial_sum = jnp.sum(grad_wide * moved(src, col_tap * spacing // step, 1), axis=(0, 1))
                rows.append(jnp.sum(partial_sum, axis=0))
        for row_tap in (-1, 0, 1):
            row_moved = moved(grad_wide, -row_tap * spacing // step, 2)
            for col_tap in (-1, 0, 1):
                local = local + taps_all[branch, 3 * (row_tap + 1) + col_tap + 1] * moved(
                    row_moved, -col_tap * spacing // step, 1
                )
        kernel_terms.append(jnp.stack(rows))
    local = total_grad.reshape(current.shape) + plain_back.reshape(current.shape) + local
    return branch_grads, local, (jnp.stack(kernel_terms), jnp.stack(point_terms), proj_term)


def butterfly_sum(vec, axes, count):
    me = lax.axis_index(axes)
    buf = vec
    steps = count.bit_length() - 1
    for k in range(steps):
        bit = 1 << k
        half = buf.shape[0] // 2
        upper = (me // bit) % 2
        keep = lax.dynamic_slice_in_dim(buf, upper * half, half)
        send = lax.dynamic_slice_in_dim(buf, (1 - upper) * half, half)
        got = lax.ppermute(send, axes, [(i, i ^ bit) for i in range(count)])
        buf = keep + got
    for k in reversed(range(steps)):
        bit = 1 << k
        got = lax.ppermute(buf, axes, [(i, i ^ bit) for i in range(count)])
        upper = (me // bit) % 2 == 1
        buf = jnp.where(upper, jnp.concatenate([got, buf]), jnp.concatenate([buf, got]))
    return buf


def to_classes(block, step, space_count):
    snaps, rows, cols = block.shape[:3]
    rest = block.shape[3:]
    split = block.reshape((snaps, rows, cols // step, step) + rest)
    order = (0, 1, 3, 2) + tuple(range(4, split.ndim))
    send = split.transpose(order).reshape((space_count, cols // step) + rest)
    got = lax.all_to_all(send, "space", 0, 0, tiled=True)
    return jnp.swapaxes(got, 0, 1)[None]


def per_device(feats, labels, class_weight, depth_kernel, point_weight, proj_weight, head_weight):
    snaps, tile_rows, width_cols, channels = feats.shape
    space_count = lax.axis_size("space")
    section_count = lax.axis_size("section")
    rep_count = lax.axis_size("rep")
    section_place = lax.axis_index("section")
    factor = loss_scale / (snaps * rep_count * tile_rows * space_count * width_cols)
    weight_table = class_weight.astype(jnp.float32)
    taps_all = depth_kernel[0].astype(jnp.float32)
    weights = (taps_all, point_weight[0], proj_weight[0], head_weight[0])
    step = tile_rows
    assert snaps * tile_rows * step == space_count and width_cols % step == 0
    assert all(spacing % step == 0 for spacing in spacings)
    start_map = to_classes(feats, step, space_count)
    label_map = to_classes(labels, step, space_count)

    head_grad = jnp.zeros((channels, 3), jnp.float32)
    saved = None
    current = start_map
    for moment in range(section_count):
        is_valid = section_place == moment
        views = row_views_of(current, step)
        result, head_term, record = forward_block(
            current, views, weights, label_map, factor, weight_table, step
        )
        head_grad = jnp.where(is_valid, head_term, head_grad)
        if saved is None:
            saved = record
        else:
            saved = jax.tree.map(lambda new, old: jnp.where(is_valid, new, old), record, saved)
        if moment < section_count - 1:
            current = recv_from(result, 0, -1)

    kernel_grad = jnp.zeros((3, 9, channels), jnp.float32)
    point_grad = jnp.zeros((4, channels, channels), jnp.float32)
    proj_grad = jnp.zeros((4 * channels, channels), jnp.float32)
    pixels = start_map.size // channels
    incoming = jnp.zeros((pixels, channels), jnp.float32)
    for moment in range(section_count):
        is_valid = section_place == section_count - 1 - moment
        branch_grads, local, terms = backward_block(saved, incoming, weights, step)
        kernel_grad = jnp.where(is_valid, terms[0], kernel_grad)
        point_grad = jnp.where(is_valid, terms[1], point_grad)
        proj_grad = jnp.where(is_valid, terms[2], proj_grad)
        if moment < section_count - 1:
            arriving = recv_from(local.astype(jnp.bfloat16), 0, 1)
            incoming = arriving.astype(jnp.float32).reshape(pixels, channels)

    parts = (kernel_grad, point_grad, proj_grad, head_grad)
    flat = jnp.concatenate([p.reshape(-1) for p in parts])
    group = space_count * rep_count
    chunk = group * 128
    padded = (flat.shape[0] + chunk - 1) // chunk * chunk
    flat = jnp.pad(flat, (0, padded - flat.shape[0]))
    total = butterfly_sum(flat, ("space", "rep"), group)
    outs = []
    start = 0
    for p in parts:
        outs.append(total[start : start + p.size].reshape((1,) + p.shape))
        start += p.size
    return tuple(outs)


def solution(mesh):
    placed = (
        P("rep", "space", None, None),
        P("rep", "space", None),
        P(),
        P("section", None, None, None),
        P("section", None, None, None),
        P("section", None, None),
        P("section", None, None),
    )
    return jax.shard_map(
        per_device,
        mesh=mesh,
        in_specs=placed,
        out_specs=(
            P("section", None, None, None),
            P("section", None, None, None),
            P("section", None, None),
            P("section", None, None),
        ),
        check_vma=False,
    )
```

```python
import jax
import jax.numpy as jnp
from jax import lax
from jax.sharding import PartitionSpec as P

spacings = (12, 24, 36)
loss_scale = 256.0


def recv_from(block, space_by, section_by):
    n_space = lax.axis_size("space")
    n_section = lax.axis_size("section")
    route = []
    for i in range(n_space):
        for s in range(n_section):
            si, ss = i + space_by, s + section_by
            if 0 <= si < n_space and 0 <= ss < n_section:
                route.append((si * n_section + ss, i * n_section + s))
    return lax.ppermute(block, ("space", "section"), route)


def moved(source, offset, axis_dim):
    length = source.shape[axis_dim]
    if abs(offset) >= length:
        return jnp.zeros_like(source)
    widths = [(0, 0)] * source.ndim
    widths[axis_dim] = (max(-offset, 0), max(offset, 0))
    padded = jnp.pad(source, widths)
    begin_at = max(offset, 0)
    return lax.slice_in_dim(padded, begin_at, begin_at + length, axis=axis_dim)


def matmul(first_op, second_op):
    return jnp.dot(first_op, second_op, preferred_element_type=jnp.float32)


def matmul_trans(first_op, second_op):
    return lax.dot_general(
        first_op, second_op, (((1,), (1,)), ((), ())), preferred_element_type=jnp.float32
    )


def outer(first_op, second_op):
    return lax.dot_general(
        first_op, second_op, (((0,), (0,)), ((), ())), preferred_element_type=jnp.float32
    )


def row_views_of(block, step):
    return [{a: moved(block, a * spacing // step, 2) for a in (-1, 1)} for spacing in spacings]


def forward_block(current, views, weights, label_tile, factor, weight_table, step):
    taps_all, point_mats, proj_mat, head_mat = weights
    snaps, tile_rows, width_cols, channels = current.shape
    pixels = snaps * tile_rows * width_cols
    plain_in = current.astype(jnp.float32)
    branch_maps = []
    for branch, spacing in enumerate(spacings):
        running = jnp.zeros(current.shape, jnp.float32)
        for row_tap in (-1, 0, 1):
            src = plain_in if row_tap == 0 else views[branch][row_tap].astype(jnp.float32)
            for col_tap in (-1, 0, 1):
                running = running + taps_all[branch, 3 * (row_tap + 1) + col_tap + 1] * moved(
                    src, col_tap * spacing // step, 1
                )
        branch_maps.append(running.astype(jnp.bfloat16))
    flat_in = current.reshape(pixels, channels)
    pre_acts = [matmul(branch_maps[b].reshape(pixels, channels), point_mats[b]) for b in range(3)]
    pre_acts.append(matmul(flat_in, point_mats[3]))
    joined = jnp.concatenate(
        [jnp.maximum(pre_act, 0.0).astype(jnp.bfloat16) for pre_act in pre_acts], axis=1
    )
    mixed_pre = matmul(joined, proj_mat)
    result = (flat_in.astype(jnp.float32) + jnp.maximum(mixed_pre, 0.0)).astype(jnp.bfloat16)
    logits = matmul(result, head_mat)
    class_ids = jnp.arange(3, dtype=jnp.int32)
    label_flat = label_tile.reshape(pixels, 1)
    onehot = (label_flat == class_ids[None, :]).astype(jnp.float32)
    pixel_weight = jnp.sum(onehot * weight_table[None, :], axis=1)
    chances = jax.nn.softmax(logits, axis=1)
    head_delta = ((factor * pixel_weight)[:, None] * (chances - onehot)).astype(jnp.bfloat16)
    head_term = outer(result, head_delta)
    from_head = matmul_trans(head_delta, head_mat)
    view_list = tuple(views[b][a] for b in range(3) for a in (-1, 1))
    record = (current, view_list, tuple(branch_maps), joined, mixed_pre, from_head)
    return result.reshape(current.shape), head_term, record


def backward_block(record, incoming, weights, step):
    taps_all, point_mats, proj_mat, head_mat = weights
    current, view_list, branch_maps, joined, mixed_pre, from_head = record
    snaps, tile_rows, width_cols, channels = current.shape
    pixels = snaps * tile_rows * width_cols
    total_grad = from_head + incoming
    gate_mixed = jnp.where(mixed_pre > 0, total_grad, 0.0).astype(jnp.bfloat16)
    proj_term = outer(joined, gate_mixed)
    back_joined = matmul_trans(gate_mixed, proj_mat)
    gate_joined = jnp.where(joined > 0, back_joined, 0.0).astype(jnp.bfloat16)
    flat_in = current.reshape(pixels, channels)
    point_terms = []
    branch_grads = []
    for branch in range(3):
        part_grad = gate_joined[:, branch * channels : (branch + 1) * channels]
        point_terms.append(outer(branch_maps[branch].reshape(pixels, channels), part_grad))
        branch_grads.append(
            matmul_trans(part_grad, point_mats[branch]).astype(jnp.bfloat16).reshape(current.shape)
        )
    part_grad = gate_joined[:, 3 * channels :]
    point_terms.append(outer(flat_in, part_grad))
    plain_back = matmul_trans(part_grad, point_mats[3])
    plain_in = current.astype(jnp.float32)
    local = jnp.zeros(current.shape, jnp.float32)
    kernel_terms = []
    for branch, spacing in enumerate(spacings):
        grad_wide = branch_grads[branch].astype(jnp.float32)
        rows = []
        for row_tap in (-1, 0, 1):
            if row_tap == 0:
                src = plain_in
            else:
                src = view_list[2 * branch + (0 if row_tap < 0 else 1)].astype(jnp.float32)
            for col_tap in (-1, 0, 1):
                partial_sum = jnp.sum(grad_wide * moved(src, col_tap * spacing // step, 1), axis=(0, 1))
                rows.append(jnp.sum(partial_sum, axis=0))
        for row_tap in (-1, 0, 1):
            row_moved = moved(grad_wide, -row_tap * spacing // step, 2)
            for col_tap in (-1, 0, 1):
                local = local + taps_all[branch, 3 * (row_tap + 1) + col_tap + 1] * moved(
                    row_moved, -col_tap * spacing // step, 1
                )
        kernel_terms.append(jnp.stack(rows))
    local = total_grad.reshape(current.shape) + plain_back.reshape(current.shape) + local
    return branch_grads, local, (jnp.stack(kernel_terms), jnp.stack(point_terms), proj_term)


def butterfly_sum(vec, axes, count):
    me = lax.axis_index(axes)
    buf = vec
    steps = count.bit_length() - 1
    for k in range(steps):
        bit = 1 << k
        half = buf.shape[0] // 2
        upper = (me // bit) % 2
        keep = lax.dynamic_slice_in_dim(buf, upper * half, half)
        send = lax.dynamic_slice_in_dim(buf, (1 - upper) * half, half)
        got = lax.ppermute(send, axes, [(i, i ^ bit) for i in range(count)])
        buf = keep + got
    for k in reversed(range(steps)):
        bit = 1 << k
        got = lax.ppermute(buf, axes, [(i, i ^ bit) for i in range(count)])
        upper = (me // bit) % 2 == 1
        buf = jnp.where(upper, jnp.concatenate([got, buf]), jnp.concatenate([buf, got]))
    return buf


def to_classes(block, step, space_count):
    snaps, rows, cols = block.shape[:3]
    rest = block.shape[3:]
    split = block.reshape((snaps, rows, cols // step, step) + rest)
    order = (0, 1, 3, 2) + tuple(range(4, split.ndim))
    send = split.transpose(order).reshape((space_count, cols // step) + rest)
    got = lax.all_to_all(send, "space", 0, 0, tiled=True)
    return jnp.swapaxes(got, 0, 1)[None]


def to_classes_both(feats, labels, step, space_count):
    snaps, rows, cols, channels = feats.shape
    width = cols // step
    f = feats.reshape(snaps, rows, width, step, channels).transpose(0, 1, 3, 2, 4)
    f = f.reshape(space_count, width, channels)
    l = labels.reshape(snaps, rows, width, step).transpose(0, 1, 3, 2)
    l = l.reshape(space_count, 1, width).astype(jnp.bfloat16)
    l = jnp.pad(l, ((0, 0), (0, 0), (0, channels - width)))
    got = lax.all_to_all(jnp.concatenate([f, l], axis=1), "space", 0, 0, tiled=True)
    feat_map = jnp.swapaxes(got[:, :width], 0, 1)[None]
    label_map = jnp.swapaxes(got[:, width, :width], 0, 1)[None].astype(jnp.int32)
    return feat_map, label_map


def per_device(feats, labels, class_weight, depth_kernel, point_weight, proj_weight, head_weight):
    snaps, tile_rows, width_cols, channels = feats.shape
    space_count = lax.axis_size("space")
    section_count = lax.axis_size("section")
    rep_count = lax.axis_size("rep")
    section_place = lax.axis_index("section")
    factor = loss_scale / (snaps * rep_count * tile_rows * space_count * width_cols)
    weight_table = class_weight.astype(jnp.float32)
    taps_all = depth_kernel[0].astype(jnp.float32)
    weights = (taps_all, point_weight[0], proj_weight[0], head_weight[0])
    step = tile_rows
    assert snaps * tile_rows * step == space_count and width_cols % step == 0
    assert all(spacing % step == 0 for spacing in spacings)
    start_map, label_map = to_classes_both(feats, labels, step, space_count)

    head_grad = jnp.zeros((channels, 3), jnp.float32)
    saved = None
    current = start_map
    for moment in range(section_count):
        is_valid = section_place == moment
        views = row_views_of(current, step)
        result, head_term, record = forward_block(
            current, views, weights, label_map, factor, weight_table, step
        )
        head_grad = jnp.where(is_valid, head_term, head_grad)
        if saved is None:
            saved = record
        else:
            saved = jax.tree.map(lambda new, old: jnp.where(is_valid, new, old), record, saved)
        if moment < section_count - 1:
            current = recv_from(result, 0, -1)

    kernel_grad = jnp.zeros((3, 9, channels), jnp.float32)
    point_grad = jnp.zeros((4, channels, channels), jnp.float32)
    proj_grad = jnp.zeros((4 * channels, channels), jnp.float32)
    pixels = start_map.size // channels
    incoming = jnp.zeros((pixels, channels), jnp.float32)
    for moment in range(section_count):
        is_valid = section_place == section_count - 1 - moment
        branch_grads, local, terms = backward_block(saved, incoming, weights, step)
        kernel_grad = jnp.where(is_valid, terms[0], kernel_grad)
        point_grad = jnp.where(is_valid, terms[1], point_grad)
        proj_grad = jnp.where(is_valid, terms[2], proj_grad)
        if moment < section_count - 1:
            arriving = recv_from(local.astype(jnp.bfloat16), 0, 1)
            incoming = arriving.astype(jnp.float32).reshape(pixels, channels)

    parts = (kernel_grad, point_grad, proj_grad, head_grad)
    flat = jnp.concatenate([p.reshape(-1) for p in parts])
    group = space_count * rep_count
    chunk = group * 128
    padded = (flat.shape[0] + chunk - 1) // chunk * chunk
    flat = jnp.pad(flat, (0, padded - flat.shape[0]))
    total = butterfly_sum(flat, ("space", "rep"), group)
    outs = []
    start = 0
    for p in parts:
        outs.append(total[start : start + p.size].reshape((1,) + p.shape))
        start += p.size
    return tuple(outs)


def solution(mesh):
    placed = (
        P("rep", "space", None, None),
        P("rep", "space", None),
        P(),
        P("section", None, None, None),
        P("section", None, None, None),
        P("section", None, None),
        P("section", None, None),
    )
    return jax.shard_map(
        per_device,
        mesh=mesh,
        in_specs=placed,
        out_specs=(
            P("section", None, None, None),
            P("section", None, None, None),
            P("section", None, None),
            P("section", None, None),
        ),
        check_vma=False,
    )
```
